768 devices in a mesh: shard: 16 (over x_hi, y), rep: 48 (over x_lo, z, core).
Axes of the slice: x: 4 (x_hi: 2, x_lo: 2; x = x_hi * 2 + x_lo), y: 8, z: 12, core: 2. Of those that a mesh axis runs over, the one named last changes fastest.
Arguments:
- hidden_act: bfloat16 [1536, 196, 3072], P(('shard', 'rep')), may hold values from -24 to 24
- out_grad: bfloat16 [1536, 196, 768], P(('shard', 'rep')), may hold values from -0.23925781 to 0.23925781
- grn_gamma: float32 [3072], replicated, may hold values from -4 to 4
- grn_beta: float32 [3072], replicated, may hold values from -4 to 4
- master: float32 [3072, 768], P('shard'), may hold values from -0.109375 to 0.109375
- moment_one: float32 [3072, 768], P('shard'), may hold values from -5 to 5
- moment_two: float32 [3072, 768], P('shard'), may hold values from 0.1 to 2
Outputs:
- new_master: float32 [3072, 768], P('shard')
- new_moment_one: float32 [3072, 768], P('shard')
- new_moment_two: float32 [3072, 768], P('shard')
- weights: bfloat16 [3072, 768], P(None, 'rep')
The draws below stay inside these ranges and needn't reach their ends.
All inputs are finite; a program needn't handle non-finite values.
Results may differ from the reference program's by a relative error of at most 0.02.
Values may be sent and summed in bfloat16 or wider, within the bound.
No kernel may reach another device: no remote copies, remote signals or barrier semaphores. Data moves between devices by JAX's collectives and lax.ppermute only.
A program may use at most 64 MiB of HBM per device.

```python
import math
import jax
import jax.numpy as jnp
from jax import lax

HID = 3072
CW = 768
POS = 196
IMG_DEV = 2
IMAGES = 1536
N_SHARD = 16
N_REP = 48


def strengthened(array, key, source, target, shards_of, factor):
    owner, partner = [(jnp.arange(array.shape[position]) // (array.shape[position] // shards_of)).reshape([-1 if axis == position else 1 for axis in range(array.ndim)]) for position in (source, target)]
    chosen = jax.random.permutation(key, shards_of)[partner]
    strong = (owner == chosen) | (owner == (partner + shards_of // 2) % shards_of)
    return jnp.where(strong, factor * array, array)


def steps_of(key, dims, pieces, smallest, largest):
    factor_of, own = 1.0, jax.random.fold_in(key, 6)
    for position, shards_of in pieces:
        heights = jnp.exp(jax.random.uniform(jax.random.fold_in(own, position), (shards_of,), jnp.float32, smallest / len(pieces), largest / len(pieces)))
        factor_of = factor_of * jnp.repeat(heights, dims[position] // shards_of).reshape([-1 if axis == position else 1 for axis in range(len(dims))])
    return factor_of


def centred(rng, dims, spread, most, shards=(), dtype=jnp.bfloat16):
    entries = spread * jax.random.normal(rng, dims, jnp.float32)
    if shards:
        entries = entries * steps_of(rng, dims, shards, -0.22, 0.18)
    return jnp.clip(entries, -most, most).astype(dtype)


def bell_draw_with(rng, dims, spread, bound, split, heavy, dtype=jnp.bfloat16):
    array = spread * jax.random.normal(rng, dims, jnp.float32)
    if split:
        array = array * steps_of(rng, dims, split, -0.22, 0.18)
    return jnp.clip(strengthened(array, jax.random.fold_in(rng, 3), *heavy), -bound, bound).astype(dtype)


def setup_inputs(seed: int = 0) -> dict:
    key_of = jax.random.split(jax.random.key(seed), 8)
    return {
        "hidden_act": bell_draw_with(key_of[0], (IMAGES, POS, HID), 1.0, 24.0, ((0, 768),), (0, 2, 768, 6.0)),
        "out_grad": centred(key_of[1], (IMAGES, POS, CW), 0.04, 0.23925781, ((0, 768),)),
        "grn_gamma": centred(key_of[2], (HID,), 1.0, 4.0, (), jnp.float32),
        "grn_beta": centred(key_of[3], (HID,), 1.0, 4.0, (), jnp.float32),
        "master": centred(key_of[4], (HID, CW), HID ** -0.5, 0.109375, ((0, 16),), jnp.float32),
        "moment_one": centred(key_of[5], (HID, CW), 1.0, 5.0, ((0, 16),), jnp.float32),
        "moment_two": jnp.clip(jnp.exp(math.log(2.0) - 2.9957323 * jax.random.uniform(key_of[6], (HID, CW), jnp.float32) ** steps_of(key_of[6], (HID, CW), ((0, 16),), -0.2, 0.2)), 0.1, 2.0),
    }


learn_rate = 0.001
beta_one = 0.9
beta_two = 0.999
adam_eps = 1e-08
decay_rate = 0.05
step_count = 10

def grn_forward(images, grn_gamma, grn_beta):
    values = images.astype(jnp.float32)
    spatial_norm = jnp.sqrt(lax.optimization_barrier(jnp.sum(values * values, axis=1)))
    ratio = spatial_norm / (lax.optimization_barrier(jnp.mean(spatial_norm, axis=1, keepdims=True)) + 1e-06)
    grn_out = grn_gamma * (values * ratio[:, None, :]) + grn_beta + values
    return grn_out.astype(jnp.bfloat16)

def reference(hidden_act, out_grad, grn_gamma, grn_beta, master, moment_one, moment_two):
    devices = N_SHARD * N_REP
    act_blocks = hidden_act.reshape(devices, IMG_DEV, POS, HID)
    grad_blocks = out_grad.reshape(devices, IMG_DEV * POS, CW)

    def accumulate(total, pair):
        images, cots = pair
        grn_out = grn_forward(images, grn_gamma, grn_beta).reshape(IMG_DEV * POS, HID)
        term = lax.dot_general(grn_out, cots, (((0,), (0,)), ((), ())), preferred_element_type=jnp.float32)
        term = lax.optimization_barrier(term.astype(jnp.bfloat16))
        return (total + term.astype(jnp.float32), None)
    grad, _ = lax.scan(accumulate, jnp.zeros((HID, CW), jnp.float32), (act_blocks, grad_blocks))
    new_moment_one = beta_one * moment_one + (1.0 - beta_one) * grad
    new_moment_two = beta_two * moment_two + (1.0 - beta_two) * grad * grad
    corrected_one = new_moment_one / (1.0 - beta_one ** step_count)
    corrected_two = new_moment_two / (1.0 - beta_two ** step_count)
    update = corrected_one / (jnp.sqrt(corrected_two) + adam_eps) + decay_rate * master
    new_master = master - learn_rate * update
    return (new_master, new_moment_one, new_moment_two, new_master.astype(jnp.bfloat16))
```

```python
import jax
import jax.numpy as jnp
import numpy as np
from jax import lax
from jax.sharding import Mesh
from jax.sharding import PartitionSpec as P

learn_rate = 0.001
beta_one = 0.9
beta_two = 0.999
adam_eps = 1e-08
decay_rate = 0.05
step_count = 10
CORES = 2
SWAP = [(0, 1), (1, 0)]


def grn_forward(images, grn_gamma, grn_beta):
    values = images.astype(jnp.float32)
    spatial_norm = jnp.sqrt(jnp.sum(values * values, axis=1))
    ratio = spatial_norm / (jnp.mean(spatial_norm, axis=1, keepdims=True) + 1e-06)
    grn_out = grn_gamma * (values * ratio[:, None, :]) + grn_beta + values
    return grn_out.astype(jnp.bfloat16)


def by_core(core, mine, other):
    return jnp.where(core == 0, jnp.concatenate([mine, other], 1), jnp.concatenate([other, mine], 1))


def body(hidden_act, out_grad, grn_gamma, grn_beta, master, moment_one, moment_two):
    images, positions, hidden = hidden_act.shape
    channels = out_grad.shape[2]
    flat_rows = grn_forward(hidden_act, grn_gamma, grn_beta).reshape(images * positions, hidden)
    flat_grads = out_grad.reshape(images * positions, channels)
    term = lax.dot_general(
        flat_rows, flat_grads, (((0,), (0,)), ((), ())), preferred_element_type=jnp.float32
    ).astype(jnp.bfloat16)
    core = lax.axis_index("c")
    half = channels // CORES
    mine = lax.dynamic_slice_in_dim(term, core * half, half, 1)
    other = lax.dynamic_slice_in_dim(term, (1 - core) * half, half, 1)
    chip = mine.astype(jnp.float32) + lax.ppermute(other, "c", SWAP).astype(jnp.float32)
    n_shard = lax.axis_size("shard")
    block = hidden // n_shard
    pieces = lax.all_to_all(
        chip.astype(jnp.bfloat16).reshape(n_shard, block, half), "shard", 0, 0, tiled=True
    )
    part = jnp.sum(pieces.astype(jnp.float32), axis=0)
    n_rq = lax.axis_size("rq")
    sub = block // n_rq
    pieces2 = lax.all_to_all(part.reshape(n_rq, sub, half), "rq", 0, 0, tiled=True)
    grad_sub = jnp.sum(pieces2, axis=0)
    grad_half = lax.all_gather(grad_sub, "rq", axis=0, tiled=True)
    grad = by_core(core, grad_half, lax.ppermute(grad_half, "c", SWAP))
    new_moment_one = beta_one * moment_one + (1.0 - beta_one) * grad
    new_moment_two = beta_two * moment_two + (1.0 - beta_two) * grad * grad
    corrected_one = new_moment_one / (1.0 - beta_one**step_count)
    corrected_two = new_moment_two / (1.0 - beta_two**step_count)
    update = corrected_one / (jnp.sqrt(corrected_two) + adam_eps) + decay_rate * master
    new_master = master - learn_rate * update
    n_rep = n_rq * CORES
    own_width = channels // n_rep
    own_start = (lax.axis_index("rq") * CORES + core) * own_width
    own_columns = lax.dynamic_slice_in_dim(new_master.astype(jnp.bfloat16), own_start, own_width, 1)
    weights = lax.all_gather(own_columns, "shard", axis=0, tiled=True)
    return (new_master, new_moment_one, new_moment_two, weights)


def solution(mesh):
    n_shard, n_rep = mesh.shape["shard"], mesh.shape["rep"]
    devices = np.asarray(mesh.devices).reshape(n_shard, n_rep // CORES, CORES)
    fine = Mesh(devices, ("shard", "rq", "c"))
    rows = ("shard", "rq", "c")
    in_specs = (
        P(rows, None, None),
        P(rows, None, None),
        P(),
        P(),
        P("shard", None),
        P("shard", None),
        P("shard", None),
    )
    out_specs = (P("shard", None), P("shard", None), P("shard", None), P(None, ("rq", "c")))
    return jax.shard_map(body, mesh=fine, in_specs=in_specs, out_specs=out_specs, check_vma=False)
```

```python
import jax
import jax.numpy as jnp
import numpy as np
from jax import lax
from jax.sharding import Mesh
from jax.sharding import PartitionSpec as P

learn_rate = 0.001
beta_one = 0.9
beta_two = 0.999
adam_eps = 1e-08
decay_rate = 0.05
step_count = 10
CORES = 2
SWAP = [(0, 1), (1, 0)]


def grn_forward(images, grn_gamma, grn_beta):
    values = images.astype(jnp.float32)
    spatial_norm = jnp.sqrt(jnp.sum(values * values, axis=1))
    ratio = spatial_norm / (jnp.mean(spatial_norm, axis=1, keepdims=True) + 1e-06)
    grn_out = grn_gamma * (values * ratio[:, None, :]) + grn_beta + values
    return grn_out.astype(jnp.bfloat16)


def by_core(core, mine, other):
    return jnp.where(core == 0, jnp.concatenate([mine, other], 1), jnp.concatenate([other, mine], 1))


def body(hidden_act, out_grad, grn_gamma, grn_beta, master, moment_one, moment_two):
    images, positions, hidden = hidden_act.shape
    channels = out_grad.shape[2]
    flat_rows = grn_forward(hidden_act, grn_gamma, grn_beta).reshape(images * positions, hidden)
    flat_grads = out_grad.reshape(images * positions, channels)
    term = lax.dot_general(
        flat_rows, flat_grads, (((0,), (0,)), ((), ())), preferred_element_type=jnp.float32
    ).astype(jnp.bfloat16)
    core = lax.axis_index("c")
    half = channels // CORES
    mine = lax.dynamic_slice_in_dim(term, core * half, half, 1)
    other = lax.dynamic_slice_in_dim(term, (1 - core) * half, half, 1)
    chip = mine.astype(jnp.float32) + lax.ppermute(other, "c", SWAP).astype(jnp.float32)
    n_shard = lax.axis_size("shard")
    block = hidden // n_shard
    pieces = lax.all_to_all(
        chip.astype(jnp.bfloat16).reshape(n_shard, block, half), "shard", 0, 0, tiled=True
    )
    part = jnp.sum(pieces.astype(jnp.float32), axis=0)
    x_lo = lax.axis_index("xl")
    rows_half = block // 2
    mine_rows = lax.dynamic_slice_in_dim(part, x_lo * rows_half, rows_half, 0)
    other_rows = lax.dynamic_slice_in_dim(part, (1 - x_lo) * rows_half, rows_half, 0)
    part_half = mine_rows + lax.ppermute(other_rows, "xl", SWAP)
    n_z = lax.axis_size("z")
    sub = rows_half // n_z
    pieces2 = lax.all_to_all(part_half.reshape(n_z, sub, half), "z", 0, 0, tiled=True)
    grad_sub = jnp.sum(pieces2, axis=0)
    spread = jnp.broadcast_to(grad_sub[None], (n_z, sub, half))
    grad_quarter = lax.all_to_all(spread, "z", 0, 0, tiled=True).reshape(rows_half, half)
    from_x = lax.ppermute(grad_quarter, "xl", SWAP)
    from_core = lax.ppermute(grad_quarter, "c", SWAP)
    from_both = lax.ppermute(grad_quarter, ("xl", "c"), [(0, 3), (3, 0), (1, 2), (2, 1)])
    own_half = by_core(core, grad_quarter, from_core)
    far_half = by_core(core, from_x, from_both)
    grad = jnp.where(x_lo == 0, jnp.concatenate([own_half, far_half], 0), jnp.concatenate([far_half, own_half], 0))
    new_moment_one = beta_one * moment_one + (1.0 - beta_one) * grad
    new_moment_two = beta_two * moment_two + (1.0 - beta_two) * grad * grad
    corrected_one = new_moment_one / (1.0 - beta_one**step_count)
    corrected_two = new_moment_two / (1.0 - beta_two**step_count)
    update = corrected_one / (jnp.sqrt(corrected_two) + adam_eps) + decay_rate * master
    new_master = master - learn_rate * update
    n_rep = lax.axis_size(("xl", "z", "c"))
    own_width = channels // n_rep
    own_start = lax.axis_index(("xl", "z", "c")) * own_width
    own_columns = lax.dynamic_slice_in_dim(new_master.astype(jnp.bfloat16), own_start, own_width, 1)
    spread_cols = jnp.broadcast_to(own_columns[None], (n_shard, block, own_width))
    weights = lax.all_to_all(spread_cols, "shard", 0, 0, tiled=True).reshape(hidden, own_width)
    return (new_master, new_moment_one, new_moment_two, weights)


def solution(mesh):
    n_shard, n_rep = mesh.shape["shard"], mesh.shape["rep"]
    x_lo = 2
    devices = np.asarray(mesh.devices).reshape(n_shard, x_lo, n_rep // (x_lo * CORES), CORES)
    fine = Mesh(devices, ("shard", "xl", "z", "c"))
    rows = ("shard", "xl", "z", "c")
    in_specs = (
        P(rows, None, None),
        P(rows, None, None),
        P(),
        P(),
        P("shard", None),
        P("shard", None),
        P("shard", None),
    )
    out_specs = (P("shard", None), P("shard", None), P("shard", None), P(None, ("xl", "z", "c")))
    return jax.shard_map(body, mesh=fine, in_specs=in_specs, out_specs=out_specs, check_vma=False)
```

```python
import jax
import jax.numpy as jnp
import numpy as np
from jax import lax
from jax.sharding import Mesh
from jax.sharding import PartitionSpec as P

learn_rate = 0.001
beta_one = 0.9
beta_two = 0.999
adam_eps = 1e-08
decay_rate = 0.05
step_count = 10
CORES = 2
SWAP = [(0, 1), (1, 0)]


def grn_forward(images, grn_gamma, grn_beta):
    values = images.astype(jnp.float32)
    spatial_norm = jnp.sqrt(jnp.sum(values * values, axis=1))
    ratio = spatial_norm / (jnp.mean(spatial_norm, axis=1, keepdims=True) + 1e-06)
    grn_out = grn_gamma * (values * ratio[:, None, :]) + grn_beta + values
    return grn_out.astype(jnp.bfloat16)


def by_core(core, mine, other):
    return jnp.where(core == 0, jnp.concatenate([mine, other], 1), jnp.concatenate([other, mine], 1))


def body(hidden_act, out_grad, grn_gamma, grn_beta, master, moment_one, moment_two):
    images, positions, hidden = hidden_act.shape
    channels = out_grad.shape[2]
    flat_rows = grn_forward(hidden_act, grn_gamma, grn_beta).reshape(images * positions, hidden)
    flat_grads = out_grad.reshape(images * positions, channels)
    core = lax.axis_index("c")
    half = channels // CORES

    def term_of(start):
        cols = lax.dynamic_slice_in_dim(flat_grads, start, half, 1)
        return lax.dot_general(
            flat_rows, cols, (((0,), (0,)), ((), ())), preferred_element_type=jnp.float32
        ).astype(jnp.bfloat16)

    sent = lax.ppermute(term_of((1 - core) * half), "c", SWAP)
    chip = term_of(core * half).astype(jnp.float32) + sent.astype(jnp.float32)
    n_shard = lax.axis_size(("xh", "y"))
    n_xh = lax.axis_size("xh")
    n_y = lax.axis_size("y")
    block = hidden // n_shard
    x_hi = lax.axis_index("xh")
    wide = hidden // n_xh
    keep = lax.dynamic_slice_in_dim(chip, x_hi * wide, wide, 0)
    give = lax.dynamic_slice_in_dim(chip.astype(jnp.bfloat16), (1 - x_hi) * wide, wide, 0)
    pair = keep + lax.ppermute(give, "xh", SWAP).astype(jnp.float32)
    pieces = lax.all_to_all(
        pair.astype(jnp.bfloat16).reshape(n_y, block, half), "y", 0, 0, tiled=True
    )
    part = jnp.sum(pieces.astype(jnp.float32), axis=0)
    x_lo = lax.axis_index("xl")
    rows_half = block // 2
    mine_rows = lax.dynamic_slice_in_dim(part, x_lo * rows_half, rows_half, 0)
    other_rows = lax.dynamic_slice_in_dim(part, (1 - x_lo) * rows_half, rows_half, 0)
    part_half = mine_rows + lax.ppermute(other_rows, "xl", SWAP)
    n_z = lax.axis_size("z")
    sub = rows_half // n_z
    pieces2 = lax.all_to_all(part_half.reshape(n_z, sub, half), "z", 0, 0, tiled=True)
    grad_sub = jnp.sum(pieces2, axis=0)
    spread = jnp.broadcast_to(grad_sub[None], (n_z, sub, half))
    grad_quarter = lax.all_to_all(spread, "z", 0, 0, tiled=True).reshape(rows_half, half)
    from_x = lax.ppermute(grad_quarter, "xl", SWAP)
    from_core = lax.ppermute(grad_quarter, "c", SWAP)
    from_both = lax.ppermute(grad_quarter, ("xl", "c"), [(0, 3), (3, 0), (1, 2), (2, 1)])
    own_half = by_core(core, grad_quarter, from_core)
    far_half = by_core(core, from_x, from_both)
    grad = jnp.where(x_lo == 0, jnp.concatenate([own_half, far_half], 0), jnp.concatenate([far_half, own_half], 0))
    new_moment_one = beta_one * moment_one + (1.0 - beta_one) * grad
    new_moment_two = beta_two * moment_two + (1.0 - beta_two) * grad * grad
    corrected_one = new_moment_one / (1.0 - beta_one**step_count)
    corrected_two = new_moment_two / (1.0 - beta_two**step_count)
    update = corrected_one / (jnp.sqrt(corrected_two) + adam_eps) + decay_rate * master
    new_master = master - learn_rate * update
    n_rep = lax.axis_size(("xl", "z", "c"))
    own_width = channels // n_rep
    own_start = lax.axis_index(("xl", "z", "c")) * own_width
    own_columns = lax.dynamic_slice_in_dim(new_master.astype(jnp.bfloat16), own_start, own_width, 1)
    spread_cols = jnp.broadcast_to(own_columns[None], (n_shard, block, own_width))
    weights = lax.all_to_all(spread_cols, ("xh", "y"), 0, 0, tiled=True).reshape(hidden, own_width)
    return (new_master, new_moment_one, new_moment_two, weights)


def solution(mesh):
    n_shard, n_rep = mesh.shape["shard"], mesh.shape["rep"]
    x_hi = x_lo = 2
    devices = np.asarray(mesh.devices).reshape(x_hi, n_shard // x_hi, x_lo, n_rep // (x_lo * CORES), CORES)
    fine = Mesh(devices, ("xh", "y", "xl", "z", "c"))
    rows = ("xh", "y", "xl", "z", "c")
    in_specs = (
        P(rows, None, None),
        P(rows, None, None),
        P(),
        P(),
        P(("xh", "y"), None),
        P(("xh", "y"), None),
        P(("xh", "y"), None),
    )
    out_specs = (P(("xh", "y"), None), P(("xh", "y"), None), P(("xh", "y"), None), P(None, ("xl", "z", "c")))
    return jax.shard_map(body, mesh=fine, in_specs=in_specs, out_specs=out_specs, check_vma=False)
```

```python
import jax
import jax.numpy as jnp
import numpy as np
from jax import lax
from jax.sharding import Mesh
from jax.sharding import PartitionSpec as P

learn_rate = 0.001
beta_one = 0.9
beta_two = 0.999
adam_eps = 1e-08
decay_rate = 0.05
step_count = 10
CORES = 2
SWAP = [(0, 1), (1, 0)]


def grn_forward(images, grn_gamma, grn_beta):
    values = images.astype(jnp.float32)
    spatial_norm = jnp.sqrt(jnp.sum(values * values, axis=1))
    ratio = spatial_norm / (jnp.mean(spatial_norm, axis=1, keepdims=True) + 1e-06)
    grn_out = grn_gamma * (values * ratio[:, None, :]) + grn_beta + values
    return grn_out.astype(jnp.bfloat16)


def by_core(core, mine, other):
    return jnp.where(core == 0, jnp.concatenate([mine, other], 1), jnp.concatenate([other, mine], 1))


def body(hidden_act, out_grad, grn_gamma, grn_beta, master, moment_one, moment_two):
    images, positions, hidden = hidden_act.shape
    channels = out_grad.shape[2]
    flat_rows = grn_forward(hidden_act, grn_gamma, grn_beta).reshape(images * positions, hidden)
    flat_grads = out_grad.reshape(images * positions, channels)
    term = lax.dot_general(
        flat_rows, flat_grads, (((0,), (0,)), ((), ())), preferred_element_type=jnp.float32
    ).astype(jnp.bfloat16)
    core = lax.axis_index("c")
    half = channels // CORES
    mine = lax.dynamic_slice_in_dim(term, core * half, half, 1)
    other = lax.dynamic_slice_in_dim(term, (1 - core) * half, half, 1)
    chip = mine.astype(jnp.float32) + lax.ppermute(other, "c", SWAP).astype(jnp.float32)
    n_shard = lax.axis_size("shard")
    block = hidden // n_shard
    pieces = lax.all_to_all(
        chip.astype(jnp.bfloat16).reshape(n_shard, block, half), "shard", 0, 0, tiled=True
    )
    part = jnp.sum(pieces.astype(jnp.float32), axis=0)
    x_lo = lax.axis_index("xl")
    rows_half = block // 2
    n_z = lax.axis_size("z")
    n_xz = lax.axis_size(("xl", "z"))
    sub = block // n_xz
    pieces2 = lax.all_to_all(part.reshape(n_xz, sub, half), ("xl", "z"), 0, 0, tiled=True)
    grad_sub = jnp.sum(pieces2, axis=0)
    spread = jnp.broadcast_to(grad_sub[None], (n_z, sub, half))
    grad_quarter = lax.all_to_all(spread, "z", 0, 0, tiled=True).reshape(rows_half, half)
    from_x = lax.ppermute(grad_quarter, "xl", SWAP)
    from_core = lax.ppermute(grad_quarter, "c", SWAP)
    from_both = lax.ppermute(grad_quarter, ("xl", "c"), [(0, 3), (3, 0), (1, 2), (2, 1)])
    own_half = by_core(core, grad_quarter, from_core)
    far_half = by_core(core, from_x, from_both)
    grad = jnp.where(x_lo == 0, jnp.concatenate([own_half, far_half], 0), jnp.concatenate([far_half, own_half], 0))
    new_moment_one = beta_one * moment_one + (1.0 - beta_one) * grad
    new_moment_two = beta_two * moment_two + (1.0 - beta_two) * grad * grad
    corrected_one = new_moment_one / (1.0 - beta_one**step_count)
    corrected_two = new_moment_two / (1.0 - beta_two**step_count)
    update = corrected_one / (jnp.sqrt(corrected_two) + adam_eps) + decay_rate * master
    new_master = master - learn_rate * update
    n_rep = lax.axis_size(("xl", "z", "c"))
    own_width = channels // n_rep
    own_start = lax.axis_index(("xl", "z", "c")) * own_width
    own_columns = lax.dynamic_slice_in_dim(new_master.astype(jnp.bfloat16), own_start, own_width, 1)
    spread_cols = jnp.broadcast_to(own_columns[None], (n_shard, block, own_width))
    weights = lax.all_to_all(spread_cols, "shard", 0, 0, tiled=True).reshape(hidden, own_width)
    return (new_master, new_moment_one, new_moment_two, weights)


def solution(mesh):
    n_shard, n_rep = mesh.shape["shard"], mesh.shape["rep"]
    x_lo = 2
    devices = np.asarray(mesh.devices).reshape(n_shard, x_lo, n_rep // (x_lo * CORES), CORES)
    fine = Mesh(devices, ("shard", "xl", "z", "c"))
    rows = ("shard", "xl", "z", "c")
    in_specs = (
        P(rows, None, None),
        P(rows, None, None),
        P(),
        P(),
        P("shard", None),
        P("shard", None),
        P("shard", None),
    )
    out_specs = (P("shard", None), P("shard", None), P("shard", None), P(None, ("xl", "z", "c")))
    return jax.shard_map(body, mesh=fine, in_specs=in_specs, out_specs=out_specs, check_vma=False)
```

```python
import jax
import jax.numpy as jnp
import numpy as np
from jax import lax
from jax.sharding import Mesh
from jax.sharding import PartitionSpec as P

learn_rate = 0.001
beta_one = 0.9
beta_two = 0.999
adam_eps = 1e-08
decay_rate = 0.05
step_count = 10
CORES = 2
SWAP = [(0, 1), (1, 0)]


def grn_forward(images, grn_gamma, grn_beta):
    values = images.astype(jnp.float32)
    spatial_norm = jnp.sqrt(jnp.sum(values * values, axis=1))
    ratio = spatial_norm / (jnp.mean(spatial_norm, axis=1, keepdims=True) + 1e-06)
    grn_out = grn_gamma * (values * ratio[:, None, :]) + grn_beta + values
    return grn_out.astype(jnp.bfloat16)


def by_core(core, mine, other):
    return jnp.where(core == 0, jnp.concatenate([mine, other], 1), jnp.concatenate([other, mine], 1))


def body(hidden_act, out_grad, grn_gamma, grn_beta, master, moment_one, moment_two):
    images, positions, hidden = hidden_act.shape
    channels = out_grad.shape[2]
    flat_rows = grn_forward(hidden_act, grn_gamma, grn_beta).reshape(images * positions, hidden)
    flat_grads = out_grad.reshape(images * positions, channels)
    term = lax.dot_general(
        flat_rows, flat_grads, (((0,), (0,)), ((), ())), preferred_element_type=jnp.float32
    ).astype(jnp.bfloat16)
    core = lax.axis_index("c")
    half = channels // CORES
    mine = lax.dynamic_slice_in_dim(term, core * half, half, 1)
    other = lax.dynamic_slice_in_dim(term, (1 - core) * half, half, 1)
    chip = mine.astype(jnp.float32) + lax.ppermute(other, "c", SWAP).astype(jnp.float32)
    n_shard = lax.axis_size("shard")
    block = hidden // n_shard
    pieces = lax.all_to_all(
        chip.astype(jnp.bfloat16).reshape(n_shard, block, half), "shard", 0, 0, tiled=True
    )
    part = jnp.sum(pieces.astype(jnp.float32), axis=0)
    x_lo = lax.axis_index("xl")
    rows_half = block // 2
    n_z = lax.axis_size("z")
    n_xz = lax.axis_size(("xl", "z"))
    sub = block // n_xz
    pieces2 = lax.all_to_all(
        part.astype(jnp.bfloat16).reshape(n_xz, sub, half), ("xl", "z"), 0, 0, tiled=True
    )
    grad_sub = jnp.sum(pieces2.astype(jnp.float32), axis=0)
    spread = jnp.broadcast_to(grad_sub[None], (n_z, sub, half))
    grad_quarter = lax.all_to_all(spread, "z", 0, 0, tiled=True).reshape(rows_half, half)
    from_x = lax.ppermute(grad_quarter, "xl", SWAP)
    from_core = lax.ppermute(grad_quarter, "c", SWAP)
    from_both = lax.ppermute(grad_quarter, ("xl", "c"), [(0, 3), (3, 0), (1, 2), (2, 1)])
    own_half = by_core(core, grad_quarter, from_core)
    far_half = by_core(core, from_x, from_both)
    grad = jnp.where(x_lo == 0, jnp.concatenate([own_half, far_half], 0), jnp.concatenate([far_half, own_half], 0))
    new_moment_one = beta_one * moment_one + (1.0 - beta_one) * grad
    new_moment_two = beta_two * moment_two + (1.0 - beta_two) * grad * grad
    corrected_one = new_moment_one / (1.0 - beta_one**step_count)
    corrected_two = new_moment_two / (1.0 - beta_two**step_count)
    update = corrected_one / (jnp.sqrt(corrected_two) + adam_eps) + decay_rate * master
    new_master = master - learn_rate * update
    n_rep = lax.axis_size(("xl", "z", "c"))
    own_width = channels // n_rep
    own_start = lax.axis_index(("xl", "z", "c")) * own_width
    own_columns = lax.dynamic_slice_in_dim(new_master.astype(jnp.bfloat16), own_start, own_width, 1)
    spread_cols = jnp.broadcast_to(own_columns[None], (n_shard, block, own_width))
    weights = lax.all_to_all(spread_cols, "shard", 0, 0, tiled=True).reshape(hidden, own_width)
    return (new_master, new_moment_one, new_moment_two, weights)


def solution(mesh):
    n_shard, n_rep = mesh.shape["shard"], mesh.shape["rep"]
    x_lo = 2
    devices = np.asarray(mesh.devices).reshape(n_shard, x_lo, n_rep // (x_lo * CORES), CORES)
    fine = Mesh(devices, ("shard", "xl", "z", "c"))
    rows = ("shard", "xl", "z", "c")
    in_specs = (
        P(rows, None, None),
        P(rows, None, None),
        P(),
        P(),
        P("shard", None),
        P("shard", None),
        P("shard", None),
    )
    out_specs = (P("shard", None), P("shard", None), P("shard", None), P(None, ("xl", "z", "c")))
    return jax.shard_map(body, mesh=fine, in_specs=in_specs, out_specs=out_specs, check_vma=False)
```

```python
import jax
import jax.numpy as jnp
import numpy as np
from jax import lax
from jax.sharding import Mesh
from jax.sharding import PartitionSpec as P

learn_rate = 0.001
beta_one = 0.9
beta_two = 0.999
adam_eps = 1e-08
decay_rate = 0.05
step_count = 10
CORES = 2
SWAP = [(0, 1), (1, 0)]


def grn_forward(images, grn_gamma, grn_beta):
    values = images.astype(jnp.float32)
    spatial_norm = jnp.sqrt(jnp.sum(values * values, axis=1))
    ratio = spatial_norm / (jnp.mean(spatial_norm, axis=1, keepdims=True) + 1e-06)
    grn_out = grn_gamma * (values * ratio[:, None, :]) + grn_beta + values
    return grn_out.astype(jnp.bfloat16)


def by_core(core, mine, other):
    return jnp.where(core == 0, jnp.concatenate([mine, other], 1), jnp.concatenate([other, mine], 1))


def body(hidden_act, out_grad, grn_gamma, grn_beta, master, moment_one, moment_two):
    images, positions, hidden = hidden_act.shape
    channels = out_grad.shape[2]
    grn_out = grn_forward(hidden_act, grn_gamma, grn_beta)
    term = sum(
        lax.dot_general(
            grn_out[i], out_grad[i], (((0,), (0,)), ((), ())), preferred_element_type=jnp.float32
        )
        for i in range(images)
    ).astype(jnp.bfloat16)
    core = lax.axis_index("c")
    half = channels // CORES
    mine = lax.dynamic_slice_in_dim(term, core * half, half, 1)
    other = lax.dynamic_slice_in_dim(term, (1 - core) * half, half, 1)
    chip = mine.astype(jnp.float32) + lax.ppermute(other, "c", SWAP).astype(jnp.float32)
    n_shard = lax.axis_size("shard")
    block = hidden // n_shard
    pieces = lax.all_to_all(
        chip.astype(jnp.bfloat16).reshape(n_shard, block, half), "shard", 0, 0, tiled=True
    )
    part = jnp.sum(pieces.astype(jnp.float32), axis=0)
    x_lo = lax.axis_index("xl")
    rows_half = block // 2
    n_z = lax.axis_size("z")
    n_xz = lax.axis_size(("xl", "z"))
    sub = block // n_xz
    pieces2 = lax.all_to_all(
        part.astype(jnp.bfloat16).reshape(n_xz, sub, half), ("xl", "z"), 0, 0, tiled=True
    )
    grad_sub = jnp.sum(pieces2.astype(jnp.float32), axis=0)
    spread = jnp.broadcast_to(grad_sub[None], (n_z, sub, half))
    grad_quarter = lax.all_to_all(spread, "z", 0, 0, tiled=True).reshape(rows_half, half)
    from_x = lax.ppermute(grad_quarter, "xl", SWAP)
    from_core = lax.ppermute(grad_quarter, "c", SWAP)
    from_both = lax.ppermute(grad_quarter, ("xl", "c"), [(0, 3), (3, 0), (1, 2), (2, 1)])
    own_half = by_core(core, grad_quarter, from_core)
    far_half = by_core(core, from_x, from_both)
    grad = jnp.where(x_lo == 0, jnp.concatenate([own_half, far_half], 0), jnp.concatenate([far_half, own_half], 0))
    new_moment_one = beta_one * moment_one + (1.0 - beta_one) * grad
    new_moment_two = beta_two * moment_two + (1.0 - beta_two) * grad * grad
    corrected_one = new_moment_one / (1.0 - beta_one**step_count)
    corrected_two = new_moment_two / (1.0 - beta_two**step_count)
    update = corrected_one / (jnp.sqrt(corrected_two) + adam_eps) + decay_rate * master
    new_master = master - learn_rate * update
    n_rep = lax.axis_size(("xl", "z", "c"))
    own_width = channels // n_rep
    own_start = lax.axis_index(("xl", "z", "c")) * own_width
    own_columns = lax.dynamic_slice_in_dim(new_master.astype(jnp.bfloat16), own_start, own_width, 1)
    spread_cols = jnp.broadcast_to(own_columns[None], (n_shard, block, own_width))
    weights = lax.all_to_all(spread_cols, "shard", 0, 0, tiled=True).reshape(hidden, own_width)
    return (new_master, new_moment_one, new_moment_two, weights)


def solution(mesh):
    n_shard, n_rep = mesh.shape["shard"], mesh.shape["rep"]
    x_lo = 2
    devices = np.asarray(mesh.devices).reshape(n_shard, x_lo, n_rep // (x_lo * CORES), CORES)
    fine = Mesh(devices, ("shard", "xl", "z", "c"))
    rows = ("shard", "xl", "z", "c")
    in_specs = (
        P(rows, None, None),
        P(rows, None, None),
        P(),
        P(),
        P("shard", None),
        P("shard", None),
        P("shard", None),
    )
    out_specs = (P("shard", None), P("shard", None), P("shard", None), P(None, ("xl", "z", "c")))
    return jax.shard_map(body, mesh=fine, in_specs=in_specs, out_specs=out_specs, check_vma=False)
```

```python
import jax
import jax.numpy as jnp
import numpy as np
from jax import lax
from jax.sharding import Mesh
from jax.sharding import PartitionSpec as P

learn_rate = 0.001
beta_one = 0.9
beta_two = 0.999
adam_eps = 1e-08
decay_rate = 0.05
step_count = 10
CORES = 2
SWAP = [(0, 1), (1, 0)]


def grn_forward(images, grn_gamma, grn_beta):
    values = images.astype(jnp.float32)
    spatial_norm = jnp.sqrt(jnp.sum(values * values, axis=1))
    ratio = spatial_norm / (jnp.mean(spatial_norm, axis=1, keepdims=True) + 1e-06)
    grn_out = grn_gamma * (values * ratio[:, None, :]) + grn_beta + values
    return grn_out.astype(jnp.bfloat16)


def by_core(core, mine, other):
    return jnp.where(core == 0, jnp.concatenate([mine, other], 1), jnp.concatenate([other, mine], 1))


def body(hidden_act, out_grad, grn_gamma, grn_beta, master, moment_one, moment_two):
    images, positions, hidden = hidden_act.shape
    channels = out_grad.shape[2]
    grn_out = grn_forward(hidden_act, grn_gamma, grn_beta)
    core = lax.axis_index("c")
    half = channels // CORES

    def term_of(start):
        cols = lax.dynamic_slice_in_dim(out_grad, start, half, 2)
        return sum(
            lax.dot_general(
                grn_out[i], cols[i], (((0,), (0,)), ((), ())), preferred_element_type=jnp.float32
            )
            for i in range(images)
        ).astype(jnp.bfloat16)

    sent = lax.ppermute(term_of((1 - core) * half), "c", SWAP)
    chip = term_of(core * half).astype(jnp.float32) + sent.astype(jnp.float32)
    n_shard = lax.axis_size("shard")
    block = hidden // n_shard
    pieces = lax.all_to_all(
        chip.astype(jnp.bfloat16).reshape(n_shard, block, half), "shard", 0, 0, tiled=True
    )
    part = jnp.sum(pieces.astype(jnp.float32), axis=0)
    x_lo = lax.axis_index("xl")
    rows_half = block // 2
    n_z = lax.axis_size("z")
    n_xz = lax.axis_size(("xl", "z"))
    sub = block // n_xz
    pieces2 = lax.all_to_all(
        part.astype(jnp.bfloat16).reshape(n_xz, sub, half), ("xl", "z"), 0, 0, tiled=True
    )
    grad_sub = jnp.sum(pieces2.astype(jnp.float32), axis=0)
    spread = jnp.broadcast_to(grad_sub[None], (n_z, sub, half))
    grad_quarter = lax.all_to_all(spread, "z", 0, 0, tiled=True).reshape(rows_half, half)
    from_x = lax.ppermute(grad_quarter, "xl", SWAP)
    from_core = lax.ppermute(grad_quarter, "c", SWAP)
    from_both = lax.ppermute(grad_quarter, ("xl", "c"), [(0, 3), (3, 0), (1, 2), (2, 1)])
    own_half = by_core(core, grad_quarter, from_core)
    far_half = by_core(core, from_x, from_both)
    grad = jnp.where(x_lo == 0, jnp.concatenate([own_half, far_half], 0), jnp.concatenate([far_half, own_half], 0))
    new_moment_one = beta_one * moment_one + (1.0 - beta_one) * grad
    new_moment_two = beta_two * moment_two + (1.0 - beta_two) * grad * grad
    corrected_one = new_moment_one / (1.0 - beta_one**step_count)
    corrected_two = new_moment_two / (1.0 - beta_two**step_count)
    update = corrected_one / (jnp.sqrt(corrected_two) + adam_eps) + decay_rate * master
    new_master = master - learn_rate * update
    n_rep = lax.axis_size(("xl", "z", "c"))
    own_width = channels // n_rep
    own_start = lax.axis_index(("xl", "z", "c")) * own_width
    own_columns = lax.dynamic_slice_in_dim(new_master.astype(jnp.bfloat16), own_start, own_width, 1)
    spread_cols = jnp.broadcast_to(own_columns[None], (n_shard, block, own_width))
    weights = lax.all_to_all(spread_cols, "shard", 0, 0, tiled=True).reshape(hidden, own_width)
    return (new_master, new_moment_one, new_moment_two, weights)


def solution(mesh):
    n_shard, n_rep = mesh.shape["shard"], mesh.shape["rep"]
    x_lo = 2
    devices = np.asarray(mesh.devices).reshape(n_shard, x_lo, n_rep // (x_lo * CORES), CORES)
    fine = Mesh(devices, ("shard", "xl", "z", "c"))
    rows = ("shard", "xl", "z", "c")
    in_specs = (
        P(rows, None, None),
        P(rows, None, None),
        P(),
        P(),
        P("shard", None),
        P("shard", None),
        P("shard", None),
    )
    out_specs = (P("shard", None), P("shard", None), P("shard", None), P(None, ("xl", "z", "c")))
    return jax.shard_map(body, mesh=fine, in_specs=in_specs, out_specs=out_specs, check_vma=False)
```

```python
import jax
import jax.numpy as jnp
import numpy as np
from jax import lax
from jax.sharding import Mesh
from jax.sharding import PartitionSpec as P

learn_rate = 0.001
beta_one = 0.9
beta_two = 0.999
adam_eps = 1e-08
decay_rate = 0.05
step_count = 10
CORES = 2
SWAP = [(0, 1), (1, 0)]


def grn_forward(images, grn_gamma, grn_beta):
    values = images.astype(jnp.float32)
    spatial_norm = jnp.sqrt(jnp.sum(values * values, axis=1))
    ratio = spatial_norm / (jnp.mean(spatial_norm, axis=1, keepdims=True) + 1e-06)
    grn_out = grn_gamma * (values * ratio[:, None, :]) + grn_beta + values
    return grn_out.astype(jnp.bfloat16)


def by_core(core, mine, other):
    return jnp.where(core == 0, jnp.concatenate([mine, other], 1), jnp.concatenate([other, mine], 1))


def body(hidden_act, out_grad, grn_gamma, grn_beta, master, moment_one, moment_two):
    images, positions, hidden = hidden_act.shape
    channels = out_grad.shape[2]
    grn_out = grn_forward(hidden_act, grn_gamma, grn_beta)
    core = lax.axis_index("c")
    half = channels // CORES

    def term_of(start):
        cols = lax.dynamic_slice_in_dim(out_grad, start, half, 2)
        return sum(
            lax.dot_general(
                grn_out[i], cols[i], (((0,), (0,)), ((), ())), preferred_element_type=jnp.float32
            )
            for i in range(images)
        ).astype(jnp.bfloat16)

    sent = lax.ppermute(term_of((1 - core) * half), "c", SWAP)
    chip = term_of(core * half).astype(jnp.float32) + sent.astype(jnp.float32)
    n_shard = lax.axis_size("shard")
    block = hidden // n_shard
    pieces = lax.all_to_all(
        chip.astype(jnp.bfloat16).reshape(n_shard, block, half), "shard", 0, 0, tiled=True
    )
    part = jnp.sum(pieces.astype(jnp.float32), axis=0)
    x_lo = lax.axis_index("xl")
    rows_half = block // 2
    n_z = lax.axis_size("z")
    n_xz = lax.axis_size(("xl", "z"))
    sub = block // n_xz
    pieces2 = lax.all_to_all(
        part.astype(jnp.bfloat16).reshape(n_xz, sub, half), ("xl", "z"), 0, 0, tiled=True
    )
    grad_sub = jnp.sum(pieces2.astype(jnp.float32), axis=0)
    spread = jnp.broadcast_to(grad_sub.astype(jnp.bfloat16)[None], (n_z, sub, half))
    sent_quarter = lax.all_to_all(spread, "z", 0, 0, tiled=True).reshape(rows_half, half)
    grad_quarter = sent_quarter.astype(jnp.float32)
    from_x = lax.ppermute(sent_quarter, "xl", SWAP).astype(jnp.float32)
    from_core = lax.ppermute(sent_quarter, "c", SWAP).astype(jnp.float32)
    from_both = lax.ppermute(sent_quarter, ("xl", "c"), [(0, 3), (3, 0), (1, 2), (2, 1)]).astype(jnp.float32)
    own_half = by_core(core, grad_quarter, from_core)
    far_half = by_core(core, from_x, from_both)
    grad = jnp.where(x_lo == 0, jnp.concatenate([own_half, far_half], 0), jnp.concatenate([far_half, own_half], 0))
    new_moment_one = beta_one * moment_one + (1.0 - beta_one) * grad
    new_moment_two = beta_two * moment_two + (1.0 - beta_two) * grad * grad
    corrected_one = new_moment_one / (1.0 - beta_one**step_count)
    corrected_two = new_moment_two / (1.0 - beta_two**step_count)
    update = corrected_one / (jnp.sqrt(corrected_two) + adam_eps) + decay_rate * master
    new_master = master - learn_rate * update
    n_rep = lax.axis_size(("xl", "z", "c"))
    own_width = channels // n_rep
    own_start = lax.axis_index(("xl", "z", "c")) * own_width
    own_columns = lax.dynamic_slice_in_dim(new_master.astype(jnp.bfloat16), own_start, own_width, 1)
    spread_cols = jnp.broadcast_to(own_columns[None], (n_shard, block, own_width))
    weights = lax.all_to_all(spread_cols, "shard", 0, 0, tiled=True).reshape(hidden, own_width)
    return (new_master, new_moment_one, new_moment_two, weights)


def solution(mesh):
    n_shard, n_rep = mesh.shape["shard"], mesh.shape["rep"]
    x_lo = 2
    devices = np.asarray(mesh.devices).reshape(n_shard, x_lo, n_rep // (x_lo * CORES), CORES)
    fine = Mesh(devices, ("shard", "xl", "z", "c"))
    rows = ("shard", "xl", "z", "c")
    in_specs = (
        P(rows, None, None),
        P(rows, None, None),
        P(),
        P(),
        P("shard", None),
        P("shard", None),
        P("shard", None),
    )
    out_specs = (P("shard", None), P("shard", None), P("shard", None), P(None, ("xl", "z", "c")))
    return jax.shard_map(body, mesh=fine, in_specs=in_specs, out_specs=out_specs, check_vma=False)
```
